256 devices in a mesh: gx: 8 (over x, core), gy: 32 (over y, z).
Axes of the slice: x: 4, y: 4, z: 8, core: 2. Of those that a mesh axis runs over, the one named last changes fastest.
Arguments:
- cells: bfloat16 [256, 1048576], P(None, ('gx', 'gy')), may hold values from -25 to 25
- send_index: int32 [8192, 2], P(('gx', 'gy')), may hold values from 0 to 31
- send_count: int32 [8192], P(('gx', 'gy')), may hold values from 1 to 2, as said below
- prolong_block: int32 [8192, 4], P(('gx', 'gy')), may hold values from 0 to 63, as said below
- prolong_level: int32 [8192, 4], P(('gx', 'gy')), may hold values from 0 to 3
- prolong_maps: bfloat16 [4, 128, 512], replicated, may hold values from -0.25 to 0.25
Outputs:
- factor: float32 [256, 256], replicated
- modes: float32 [128, 4194304], P(None, ('gx', 'gy'))
The draws below stay inside these ranges and needn't reach their ends.
Inputs may be any that keep to these rules, and one draw needn't show every extreme that they name: `send_count`: every sender and owner pair uses 1 to 2 slots; some pair uses all 2. `prolong_block`: the first slot feeding each brick is slot 0 of some sender, a multiple of 2.
All inputs are finite; a program needn't handle non-finite values.
Results may differ from the reference program's by a relative error of at most 0.0041.
Values may be sent and summed in bfloat16 or wider, within the bound.
No kernel may reach another device: no remote copies, remote signals or barrier semaphores. Data moves between devices by JAX's collectives and lax.ppermute only.
A program may use at most 128 MiB of HBM per device.

```python
import math
import jax
import jax.numpy as jnp
from jax import lax

S = 256
RANK = 128
BLK = 128
BRICK = 512
NB = 4
LEVELS = 4
CAP = 2
LOC_BLK = 32
BR = 32
NCELLS = 1048576
PAIRS = 8192
NBRICKS = 8192
N_GX = 8
N_GY = 32
DEVICES = 256


def draw_cells(key, part):
    key_noise, key_rough, key_phase, key_space = jax.random.split(key, 4)
    per_device = LOC_BLK * BLK
    device = (jnp.arange(NCELLS) // per_device).astype(jnp.float32)
    moment = (jnp.arange(S).astype(jnp.float32) + 0.5) / S
    noise_part = jnp.clip(jax.random.normal(key_noise, (S, NCELLS)), -4.0, 4.0)
    rising = 1.0 + 2.0 * device / max(DEVICES - 1, 1)
    decay_ratio = 0.85
    mode_count = 16
    leading = (2.0 * (1.0 - decay_ratio * decay_ratio)) ** 0.5
    phases = jax.random.uniform(key_phase, (mode_count,), minval=-math.pi, maxval=math.pi)
    space_part = jnp.clip(jax.random.normal(key_space, (mode_count, NCELLS)), -4.0, 4.0)
    summed = noise_part
    for mode_index in range(mode_count):
        amplitude = leading * decay_ratio ** mode_index
        timeline = jnp.cos(math.pi * (mode_index + 1) * moment + phases[mode_index])
        summed = summed + amplitude * timeline[:, None] * space_part[mode_index][None, :]
    rough = jnp.exp(jax.random.uniform(key_rough, (1, NCELLS), minval=-0.5, maxval=0.5))
    return jnp.clip(summed * rising[None, :] * rough, -25.0, 25.0).astype(jnp.bfloat16)


def draw_send_count(key, part):
    values = jax.random.randint(key, (DEVICES * N_GY,), 1, CAP + 1)
    return values.at[0].set(CAP).astype(jnp.int32)


def draw_prolong_block(key, part):
    key_rest, key_first = jax.random.split(jax.random.fold_in(key, 7), 2)
    values = jax.random.randint(key_rest, (NBRICKS, NB), 0, N_GY * CAP)
    first = jax.random.randint(key_first, (NBRICKS,), 0, N_GY) * CAP
    return values.at[:, 0].set(first).astype(jnp.int32)


def touch_ends(drawn, rng, smallest, high):
    dims = drawn.shape
    place = [jax.random.randint(jax.random.fold_in(rng, axis), (), 0, dims[axis]) for axis in range(len(dims))]
    drawn = drawn.at[tuple(place)].set(smallest)
    longest = dims.index(max(dims))
    place[longest] = (place[longest] + 1) % dims[longest]
    return drawn.at[tuple(place)].set(high)


def noise(rng, dims, width, reach, held_as=jnp.bfloat16):
    entries = jax.random.normal(rng, dims, jnp.float32) * width
    return jnp.minimum(jnp.maximum(entries, -reach), reach).astype(held_as)


def setup_inputs(seed: int = 0) -> dict:
    seeds = jax.random.split(jax.random.key(seed), 7)
    cells = draw_cells(jax.random.fold_in(seeds[6], 71), 0)
    send_index = touch_ends(jax.random.randint(seeds[1], (PAIRS, CAP), 0, LOC_BLK), jax.random.fold_in(seeds[1], 1), 0, LOC_BLK - 1).astype(jnp.int32)
    send_count = draw_send_count(jax.random.fold_in(seeds[6], 71), 0)
    prolong_block = draw_prolong_block(jax.random.fold_in(seeds[6], 71), 0)
    prolong_level = touch_ends(jax.random.randint(seeds[4], (NBRICKS, NB), 0, LEVELS), jax.random.fold_in(seeds[4], 1), 0, LEVELS - 1).astype(jnp.int32)
    prolong_maps = noise(seeds[5], (LEVELS, BLK, BRICK), (BLK * NB) ** -0.5, 0.25)
    return dict(cells=cells, send_index=send_index, send_count=send_count, prolong_block=prolong_block, prolong_level=prolong_level, prolong_maps=prolong_maps)


def lift(received, blocks, levels, maps):
    picked = received[:, blocks].astype(jnp.float32)
    chosen = maps[levels].astype(jnp.float32)
    lifted = jnp.einsum('sbnc,bncd->sbd', picked, chosen)
    return lifted.reshape(lifted.shape[0], -1).astype(jnp.bfloat16)

def reference(cells, send_index, send_count, prolong_block, prolong_level, prolong_maps):
    devices = N_GX * N_GY
    grid = cells.reshape(S, devices, LOC_BLK, BLK)
    index = send_index.reshape(devices, N_GY, CAP)
    count = send_count.reshape(devices, N_GY)
    blocks = prolong_block.reshape(devices, BR, NB)
    levels = prolong_level.reshape(devices, BR, NB)
    slot_ids = jnp.arange(CAP, dtype=jnp.int32)

    def bricks_of(device):
        group = device // N_GY
        column = device % N_GY
        sources = (group * N_GY + jnp.arange(N_GY, dtype=jnp.int32)).astype(jnp.int32)
        chosen = index[sources, column]
        live = slot_ids[None, :] < count[sources, column][:, None]
        data = grid[:, sources[:, None], chosen, :]
        data = data * live[None, :, :, None].astype(cells.dtype)
        received = data.reshape(S, N_GY * CAP, BLK)
        return lift(received, blocks[device], levels[device], prolong_maps)
    bricks = lax.map(bricks_of, jnp.arange(devices, dtype=jnp.int32))

    def add_gram(total, brick):
        gram = lax.dot_general(brick.astype(jnp.float32), brick.astype(jnp.float32), (((1,), (1,)), ((), ())), preferred_element_type=jnp.float32)
        return (total + gram, None)
    gram, unused = lax.scan(add_gram, jnp.zeros((S, S), jnp.float32), bricks)
    covariance = gram / (devices * BR * BRICK)
    factor = jnp.linalg.cholesky(covariance)
    head = factor[:RANK, :RANK]

    def solve_one(brick):
        return lax.linalg.triangular_solve(head, brick[:RANK].astype(jnp.float32), left_side=True, lower=True)
    modes = lax.map(solve_one, bricks)
    modes = jnp.transpose(modes, (1, 0, 2)).reshape(RANK, devices * BR * BRICK)
    return (factor, modes)
```

```python
import jax
import jax.numpy as jnp
from jax import lax
from jax.sharding import PartitionSpec as P

RANK = 128
BLK = 128


def from_partner(value, axis, bit):
    mask = 2**bit
    pairs = [(source, source ^ mask) for source in range(lax.axis_size(axis))]
    return lax.ppermute(value, axis, pairs)


def lift(received, blocks, levels, maps):
    picked = jnp.take(received, blocks, axis=1)
    chosen = jnp.take(maps, levels, axis=0)
    lifted = jnp.einsum("sbnc,bncd->sbd", picked, chosen, preferred_element_type=jnp.float32)
    return lifted.reshape(lifted.shape[0], -1).astype(jnp.bfloat16)


def combined(factor, other):
    mine = jnp.dot(factor, factor.T, precision=lax.Precision.HIGHEST)
    theirs = jnp.dot(other, other.T, precision=lax.Precision.HIGHEST)
    return jnp.linalg.cholesky(mine + theirs)


def body(cells, send_index, send_count, prolong_block, prolong_level, prolong_maps):
    snaps = cells.shape[0]
    local = cells.reshape(snaps, -1, BLK)
    peers, slots = send_index.shape
    outgoing = jnp.take(local, send_index.reshape(-1), axis=1)
    live = (jnp.arange(slots, dtype=jnp.int32)[None, :] < send_count[:, None]).reshape(-1)
    outgoing = outgoing * live[None, :, None].astype(jnp.bfloat16)
    received = lax.all_to_all(outgoing, "gy", split_axis=1, concat_axis=1, tiled=True)
    bricks = lift(received, prolong_block, prolong_level, prolong_maps)
    gram = lax.dot_general(
        bricks, bricks, (((1,), (1,)), ((), ())), preferred_element_type=jnp.float32
    )
    total_cells = lax.axis_size("gx") * lax.axis_size("gy") * bricks.shape[1]
    gram = lax.psum(gram, ("gx", "gy"))
    covariance = gram / total_cells
    factor = jnp.linalg.cholesky(covariance)
    kept = RANK
    modes = lax.linalg.triangular_solve(
        factor[:kept, :kept], bricks[:kept].astype(jnp.float32), left_side=True, lower=True
    )
    return (factor, modes)


def solution(mesh):
    in_specs = (
        P(None, ("gx", "gy")),
        P(("gx", "gy"), None),
        P(("gx", "gy")),
        P(("gx", "gy"), None),
        P(("gx", "gy"), None),
        P(),
    )
    out_specs = (P(), P(None, ("gx", "gy")))
    return jax.shard_map(body, mesh=mesh, in_specs=in_specs, out_specs=out_specs, check_vma=False)
```

```python
import jax
import jax.numpy as jnp
from jax import lax
from jax.sharding import PartitionSpec as P

RANK = 128
BLK = 128


def from_partner(value, axis, bit):
    mask = 2**bit
    pairs = [(source, source ^ mask) for source in range(lax.axis_size(axis))]
    return lax.ppermute(value, axis, pairs)


def all_sum(value):
    for axis in ("gx", "gy"):
        for bit in range(lax.axis_size(axis).bit_length() - 1):
            value = value + from_partner(value, axis, bit)
    return value


def lift(received, blocks, levels, maps):
    picked = jnp.take(received, blocks, axis=1)
    chosen = jnp.take(maps, levels, axis=0)
    lifted = jnp.einsum("sbnc,bncd->sbd", picked, chosen, preferred_element_type=jnp.float32)
    return lifted.reshape(lifted.shape[0], -1).astype(jnp.bfloat16)


def gram_of(left, right):
    return lax.dot_general(
        left, right, (((1,), (1,)), ((), ())), preferred_element_type=jnp.float32
    )


def body(cells, send_index, send_count, prolong_block, prolong_level, prolong_maps):
    snaps = cells.shape[0]
    kept = RANK
    local = cells.reshape(snaps, -1, BLK)
    peers, slots = send_index.shape
    outgoing = jnp.take(local, send_index.reshape(-1), axis=1)
    live = (jnp.arange(slots, dtype=jnp.int32)[None, :] < send_count[:, None]).reshape(-1)
    outgoing = outgoing * live[None, :, None].astype(jnp.bfloat16)
    head_out, tail_out = outgoing[:kept], outgoing[kept:]
    head_in = lax.all_to_all(head_out, "gy", split_axis=1, concat_axis=1, tiled=True)
    head_in, tail_out = lax.optimization_barrier((head_in, tail_out))
    tail_in = lax.all_to_all(tail_out, "gy", split_axis=1, concat_axis=1, tiled=True)
    total_cells = lax.axis_size("gx") * lax.axis_size("gy") * prolong_block.shape[0] * prolong_maps.shape[2]
    head = lift(head_in, prolong_block, prolong_level, prolong_maps)
    c11 = all_sum(gram_of(head, head)) / total_cells
    l11 = jnp.linalg.cholesky(c11)
    modes = lax.linalg.triangular_solve(
        l11, head.astype(jnp.float32), left_side=True, lower=True
    )
    tail_in, modes, l11 = lax.optimization_barrier((tail_in, modes, l11))
    tail = lift(tail_in, prolong_block, prolong_level, prolong_maps)
    lower = all_sum(gram_of(tail, jnp.concatenate([head, tail], axis=0))) / total_cells
    c21, c22 = lower[:, :kept], lower[:, kept:]
    l21 = lax.linalg.triangular_solve(
        l11, c21, left_side=False, lower=True, transpose_a=True
    )
    schur = c22 - jnp.dot(l21, l21.T, precision=lax.Precision.HIGHEST)
    l22 = jnp.linalg.cholesky(schur)
    factor = jnp.concatenate(
        [
            jnp.concatenate([l11, jnp.zeros((kept, snaps - kept), jnp.float32)], axis=1),
            jnp.concatenate([l21, l22], axis=1),
        ],
        axis=0,
    )
    return (factor, modes)


def solution(mesh):
    in_specs = (
        P(None, ("gx", "gy")),
        P(("gx", "gy"), None),
        P(("gx", "gy")),
        P(("gx", "gy"), None),
        P(("gx", "gy"), None),
        P(),
    )
    out_specs = (P(), P(None, ("gx", "gy")))
    return jax.shard_map(body, mesh=mesh, in_specs=in_specs, out_specs=out_specs, check_vma=False)
```

```python
import functools

import jax
import jax.numpy as jnp
from jax import lax
from jax.experimental import pallas as pl
from jax.experimental.pallas import tpu as pltpu
from jax.sharding import PartitionSpec as P

RANK = 128
BLK = 128
PER = 8


def from_partner(value, axis, bit):
    mask = 2**bit
    pairs = [(source, source ^ mask) for source in range(lax.axis_size(axis))]
    return lax.ppermute(value, axis, pairs)


def all_sum(value):
    for axis in ("gx", "gy"):
        for bit in range(lax.axis_size(axis).bit_length() - 1):
            value = value + from_partner(value, axis, bit)
    return value


def lift_kernel(feeds, brick_cells, blocks_ref, levels_ref, recv_ref, maps_ref, out_ref):
    step = pl.program_id(0)
    for i in range(PER):
        brick = step * PER + i
        acc = None
        for n in range(feeds):
            slot = blocks_ref[brick * feeds + n]
            level = levels_ref[brick * feeds + n]
            part = jnp.dot(recv_ref[slot], maps_ref[level], preferred_element_type=jnp.float32)
            acc = part if acc is None else acc + part
        out_ref[:, i * brick_cells : (i + 1) * brick_cells] = acc.astype(out_ref.dtype)


def lift(received, blocks, levels, maps):
    slots, rows, blk = received.shape
    bricks, feeds = blocks.shape
    brick_cells = maps.shape[2]
    grid_spec = pltpu.PrefetchScalarGridSpec(
        num_scalar_prefetch=2,
        grid=(bricks // PER,),
        in_specs=[
            pl.BlockSpec((slots, rows, blk), lambda s, b, l: (0, 0, 0)),
            pl.BlockSpec(maps.shape, lambda s, b, l: (0, 0, 0)),
        ],
        out_specs=pl.BlockSpec((rows, PER * brick_cells), lambda s, b, l: (0, s)),
    )
    flops = 2 * rows * blk * brick_cells * bricks * feeds
    return pl.pallas_call(
        functools.partial(lift_kernel, feeds, brick_cells),
        grid_spec=grid_spec,
        out_shape=jax.ShapeDtypeStruct((rows, bricks * brick_cells), jnp.bfloat16),
        cost_estimate=pl.CostEstimate(
            flops=flops,
            bytes_accessed=received.size * 2 + maps.size * 2 + rows * bricks * brick_cells * 2,
            transcendentals=0,
        ),
    )(blocks.reshape(-1), levels.reshape(-1), received, maps)


def gram_of(left, right):
    return lax.dot_general(
        left, right, (((1,), (1,)), ((), ())), preferred_element_type=jnp.float32
    )


def body(cells, send_index, send_count, prolong_block, prolong_level, prolong_maps):
    snaps = cells.shape[0]
    kept = RANK
    local = cells.reshape(snaps, -1, BLK).transpose(1, 0, 2)
    peers, slots = send_index.shape
    live = (jnp.arange(slots, dtype=jnp.int32)[None, :] < send_count[:, None]).reshape(-1)
    outgoing = jnp.take(local, send_index.reshape(-1), axis=0)
    outgoing = outgoing * live[:, None, None].astype(jnp.bfloat16)
    head_out, tail_out = outgoing[:, :kept], outgoing[:, kept:]
    head_in = lax.all_to_all(head_out, "gy", split_axis=0, concat_axis=0, tiled=True)
    head_in, tail_out = lax.optimization_barrier((head_in, tail_out))
    tail_in = lax.all_to_all(tail_out, "gy", split_axis=0, concat_axis=0, tiled=True)
    total_cells = lax.axis_size("gx") * lax.axis_size("gy") * prolong_block.shape[0] * prolong_maps.shape[2]
    head = lift(head_in, prolong_block, prolong_level, prolong_maps)
    c11 = all_sum(gram_of(head, head)) / total_cells
    l11 = jnp.linalg.cholesky(c11)
    inv11 = lax.linalg.triangular_solve(
        l11, jnp.eye(kept, dtype=jnp.float32), left_side=True, lower=True
    )
    inv_hi = inv11.astype(jnp.bfloat16)
    inv_lo = (inv11 - inv_hi.astype(jnp.float32)).astype(jnp.bfloat16)
    modes = jnp.dot(inv_hi, head, preferred_element_type=jnp.float32) + jnp.dot(
        inv_lo, head, preferred_element_type=jnp.float32
    )
    tail_in, modes, l11, inv11 = lax.optimization_barrier((tail_in, modes, l11, inv11))
    tail = lift(tail_in, prolong_block, prolong_level, prolong_maps)
    lower = all_sum(gram_of(tail, jnp.concatenate([head, tail], axis=0))) / total_cells
    c21, c22 = lower[:, :kept], lower[:, kept:]
    l21 = jnp.dot(c21, inv11.T, precision=lax.Precision.HIGHEST)
    schur = c22 - jnp.dot(l21, l21.T, precision=lax.Precision.HIGHEST)
    l22 = jnp.linalg.cholesky(schur)
    factor = jnp.concatenate(
        [
            jnp.concatenate([l11, jnp.zeros((kept, snaps - kept), jnp.float32)], axis=1),
            jnp.concatenate([l21, l22], axis=1),
        ],
        axis=0,
    )
    return (factor, modes)


def solution(mesh):
    in_specs = (
        P(None, ("gx", "gy")),
        P(("gx", "gy"), None),
        P(("gx", "gy")),
        P(("gx", "gy"), None),
        P(("gx", "gy"), None),
        P(),
    )
    out_specs = (P(), P(None, ("gx", "gy")))
    return jax.shard_map(body, mesh=mesh, in_specs=in_specs, out_specs=out_specs, check_vma=False)
```

```python
import functools

import jax
import jax.numpy as jnp
from jax import lax
from jax.experimental import pallas as pl
from jax.experimental.pallas import tpu as pltpu
from jax.sharding import PartitionSpec as P

RANK = 128
BLK = 128
PER = 8


def from_partner(value, axis, bit):
    mask = 2**bit
    pairs = [(source, source ^ mask) for source in range(lax.axis_size(axis))]
    return lax.ppermute(value, axis, pairs)


def all_sum(value):
    for axis in ("gx", "gy"):
        for bit in range(lax.axis_size(axis).bit_length() - 1):
            value = value + from_partner(value, axis, bit)
    return value


def lift_kernel(feeds, brick_cells, paired, blocks_ref, levels_ref, recv_ref, maps_ref, *refs):
    if paired:
        other_ref, out_ref, gram_ref = refs
    else:
        out_ref, gram_ref = refs
    step = pl.program_id(0)

    @pl.when(step == 0)
    def _():
        gram_ref[...] = jnp.zeros(gram_ref.shape, gram_ref.dtype)

    rows = out_ref.shape[0]
    for i in range(PER):
        brick = step * PER + i
        acc = None
        for n in range(feeds):
            slot = blocks_ref[brick * feeds + n]
            level = levels_ref[brick * feeds + n]
            part = jnp.dot(recv_ref[slot], maps_ref[level], preferred_element_type=jnp.float32)
            acc = part if acc is None else acc + part
        cols = slice(i * brick_cells, (i + 1) * brick_cells)
        lifted = acc.astype(out_ref.dtype)
        out_ref[:, cols] = lifted
        contract = (((1,), (1,)), ((), ()))
        if paired:
            gram_ref[:, :rows] += lax.dot_general(
                lifted, other_ref[:, cols], contract, preferred_element_type=jnp.float32
            )
            gram_ref[:, rows:] += lax.dot_general(
                lifted, lifted, contract, preferred_element_type=jnp.float32
            )
        else:
            gram_ref[...] += lax.dot_general(
                lifted, lifted, contract, preferred_element_type=jnp.float32
            )


def lift(received, blocks, levels, maps, other=None):
    slots, rows, blk = received.shape
    bricks, feeds = blocks.shape
    brick_cells = maps.shape[2]
    paired = other is not None
    in_specs = [
        pl.BlockSpec((slots, rows, blk), lambda s, b, l: (0, 0, 0)),
        pl.BlockSpec(maps.shape, lambda s, b, l: (0, 0, 0)),
    ]
    operands = [received, maps]
    gram_cols = rows
    if paired:
        in_specs.append(pl.BlockSpec((other.shape[0], PER * brick_cells), lambda s, b, l: (0, s)))
        operands.append(other)
        gram_cols = other.shape[0] + rows
    grid_spec = pltpu.PrefetchScalarGridSpec(
        num_scalar_prefetch=2,
        grid=(bricks // PER,),
        in_specs=in_specs,
        out_specs=[
            pl.BlockSpec((rows, PER * brick_cells), lambda s, b, l: (0, s)),
            pl.BlockSpec((rows, gram_cols), lambda s, b, l: (0, 0)),
        ],
    )
    cells = bricks * brick_cells
    flops = 2 * rows * blk * cells * feeds + 2 * rows * gram_cols * cells
    return pl.pallas_call(
        functools.partial(lift_kernel, feeds, brick_cells, paired),
        grid_spec=grid_spec,
        out_shape=[
            jax.ShapeDtypeStruct((rows, cells), jnp.bfloat16),
            jax.ShapeDtypeStruct((rows, gram_cols), jnp.float32),
        ],
        cost_estimate=pl.CostEstimate(
            flops=flops,
            bytes_accessed=received.size * 2 + maps.size * 2 + rows * cells * 2 * (2 if paired else 1),
            transcendentals=0,
        ),
    )(blocks.reshape(-1), levels.reshape(-1), *operands)


def body(cells, send_index, send_count, prolong_block, prolong_level, prolong_maps):
    snaps = cells.shape[0]
    kept = RANK
    local = cells.reshape(snaps, -1, BLK).transpose(1, 0, 2)
    peers, slots = send_index.shape
    live = (jnp.arange(slots, dtype=jnp.int32)[None, :] < send_count[:, None]).reshape(-1)
    outgoing = jnp.take(local, send_index.reshape(-1), axis=0)
    outgoing = outgoing * live[:, None, None].astype(jnp.bfloat16)
    head_out, tail_out = outgoing[:, :kept], outgoing[:, kept:]
    head_in = lax.all_to_all(head_out, "gy", split_axis=0, concat_axis=0, tiled=True)
    head_in, tail_out = lax.optimization_barrier((head_in, tail_out))
    tail_in = lax.all_to_all(tail_out, "gy", split_axis=0, concat_axis=0, tiled=True)
    total_cells = lax.axis_size("gx") * lax.axis_size("gy") * prolong_block.shape[0] * prolong_maps.shape[2]
    head, g11 = lift(head_in, prolong_block, prolong_level, prolong_maps)
    c11 = all_sum(g11) / total_cells
    l11 = jnp.linalg.cholesky(c11)
    inv11 = lax.linalg.triangular_solve(
        l11, jnp.eye(kept, dtype=jnp.float32), left_side=True, lower=True
    )
    inv_top = lax.reduce_precision(inv11, exponent_bits=8, mantissa_bits=7)
    inv_hi = inv_top.astype(jnp.bfloat16)
    inv_lo = (inv11 - inv_top).astype(jnp.bfloat16)
    modes = jnp.dot(inv_hi, head, preferred_element_type=jnp.float32) + jnp.dot(
        inv_lo, head, preferred_element_type=jnp.float32
    )
    tail_in, modes, l11, inv11 = lax.optimization_barrier((tail_in, modes, l11, inv11))
    tail, g2 = lift(tail_in, prolong_block, prolong_level, prolong_maps, other=head)
    lower = all_sum(g2) / total_cells
    c21, c22 = lower[:, :kept], lower[:, kept:]
    l21 = jnp.dot(c21, inv11.T, precision=lax.Precision.HIGHEST)
    schur = c22 - jnp.dot(l21, l21.T, precision=lax.Precision.HIGHEST)
    l22 = jnp.linalg.cholesky(schur)
    factor = jnp.concatenate(
        [
            jnp.concatenate([l11, jnp.zeros((kept, snaps - kept), jnp.float32)], axis=1),
            jnp.concatenate([l21, l22], axis=1),
        ],
        axis=0,
    )
    return (factor, modes)


def solution(mesh):
    in_specs = (
        P(None, ("gx", "gy")),
        P(("gx", "gy"), None),
        P(("gx", "gy")),
        P(("gx", "gy"), None),
        P(("gx", "gy"), None),
        P(),
    )
    out_specs = (P(), P(None, ("gx", "gy")))
    return jax.shard_map(body, mesh=mesh, in_specs=in_specs, out_specs=out_specs, check_vma=False)
```

```python
import functools

import jax
import jax.numpy as jnp
from jax import lax
from jax.experimental import pallas as pl
from jax.experimental.pallas import tpu as pltpu
from jax.sharding import PartitionSpec as P

RANK = 128
BLK = 128
PER = 8


def from_partner(value, axis, bit):
    mask = 2**bit
    pairs = [(source, source ^ mask) for source in range(lax.axis_size(axis))]
    return lax.ppermute(value, axis, pairs)


def all_sum(value):
    for axis in ("gx", "gy"):
        for bit in range(lax.axis_size(axis).bit_length() - 1):
            value = value + from_partner(value, axis, bit)
    return value


def lift_kernel(feeds, brick_cells, paired, blocks_ref, levels_ref, recv_ref, maps_ref, *refs):
    if paired:
        other_ref, out_ref, gram_ref = refs
    else:
        out_ref, gram_ref = refs
    step = pl.program_id(0)

    @pl.when(step == 0)
    def _():
        gram_ref[...] = jnp.zeros(gram_ref.shape, gram_ref.dtype)

    rows = out_ref.shape[0]
    for i in range(PER):
        brick = step * PER + i
        acc = None
        for n in range(feeds):
            slot = blocks_ref[brick * feeds + n]
            level = levels_ref[brick * feeds + n]
            part = jnp.dot(recv_ref[slot], maps_ref[level], preferred_element_type=jnp.float32)
            acc = part if acc is None else acc + part
        cols = slice(i * brick_cells, (i + 1) * brick_cells)
        lifted = acc.astype(out_ref.dtype)
        out_ref[:, cols] = lifted
        contract = (((1,), (1,)), ((), ()))
        if paired:
            gram_ref[:, :rows] += lax.dot_general(
                lifted, other_ref[:, cols], contract, preferred_element_type=jnp.float32
            )
            gram_ref[:, rows:] += lax.dot_general(
                lifted, lifted, contract, preferred_element_type=jnp.float32
            )
        else:
            gram_ref[...] += lax.dot_general(
                lifted, lifted, contract, preferred_element_type=jnp.float32
            )


def lift(received, blocks, levels, maps, other=None):
    slots, rows, blk = received.shape
    bricks, feeds = blocks.shape
    brick_cells = maps.shape[2]
    paired = other is not None
    in_specs = [
        pl.BlockSpec((slots, rows, blk), lambda s, b, l: (0, 0, 0)),
        pl.BlockSpec(maps.shape, lambda s, b, l: (0, 0, 0)),
    ]
    operands = [received, maps]
    gram_cols = rows
    if paired:
        in_specs.append(pl.BlockSpec((other.shape[0], PER * brick_cells), lambda s, b, l: (0, s)))
        operands.append(other)
        gram_cols = other.shape[0] + rows
    grid_spec = pltpu.PrefetchScalarGridSpec(
        num_scalar_prefetch=2,
        grid=(bricks // PER,),
        in_specs=in_specs,
        out_specs=[
            pl.BlockSpec((rows, PER * brick_cells), lambda s, b, l: (0, s)),
            pl.BlockSpec((rows, gram_cols), lambda s, b, l: (0, 0)),
        ],
    )
    cells = bricks * brick_cells
    flops = 2 * rows * blk * cells * feeds + 2 * rows * gram_cols * cells
    return pl.pallas_call(
        functools.partial(lift_kernel, feeds, brick_cells, paired),
        grid_spec=grid_spec,
        out_shape=[
            jax.ShapeDtypeStruct((rows, cells), jnp.bfloat16),
            jax.ShapeDtypeStruct((rows, gram_cols), jnp.float32),
        ],
        cost_estimate=pl.CostEstimate(
            flops=flops,
            bytes_accessed=received.size * 2 + maps.size * 2 + rows * cells * 2 * (2 if paired else 1),
            transcendentals=0,
        ),
    )(blocks.reshape(-1), levels.reshape(-1), *operands)


def body(cells, send_index, send_count, prolong_block, prolong_level, prolong_maps):
    snaps = cells.shape[0]
    kept = RANK
    local = cells.reshape(snaps, -1, BLK).transpose(1, 0, 2)
    peers, slots = send_index.shape
    live = (jnp.arange(slots, dtype=jnp.int32)[None, :] < send_count[:, None]).reshape(-1)
    outgoing = jnp.take(local, send_index.reshape(-1), axis=0)
    outgoing = outgoing * live[:, None, None].astype(jnp.bfloat16)
    head_out, tail_out = outgoing[:, :kept], outgoing[:, kept:]
    head_in = lax.all_to_all(head_out, "gy", split_axis=0, concat_axis=0, tiled=True)
    head_in, tail_out = lax.optimization_barrier((head_in, tail_out))
    tail_in = lax.all_to_all(tail_out, "gy", split_axis=0, concat_axis=0, tiled=True)
    total_cells = lax.axis_size("gx") * lax.axis_size("gy") * prolong_block.shape[0] * prolong_maps.shape[2]
    head, g11 = lift(head_in, prolong_block, prolong_level, prolong_maps)
    c11 = all_sum(g11) / total_cells
    l11 = jnp.linalg.cholesky(c11)
    tail_in, l11, head = lax.optimization_barrier((tail_in, l11, head))
    tail, g2 = lift(tail_in, prolong_block, prolong_level, prolong_maps, other=head)
    g2, l11, head = lax.optimization_barrier((g2, l11, head))
    inv11 = lax.linalg.triangular_solve(
        l11, jnp.eye(kept, dtype=jnp.float32), left_side=True, lower=True
    )
    inv_top = lax.reduce_precision(inv11, exponent_bits=8, mantissa_bits=7)
    inv_hi = inv_top.astype(jnp.bfloat16)
    inv_lo = (inv11 - inv_top).astype(jnp.bfloat16)
    modes = jnp.dot(inv_hi, head, preferred_element_type=jnp.float32) + jnp.dot(
        inv_lo, head, preferred_element_type=jnp.float32
    )
    lower = all_sum(g2) / total_cells
    c21, c22 = lower[:, :kept], lower[:, kept:]
    l21 = jnp.dot(c21, inv11.T, precision=lax.Precision.HIGHEST)
    schur = c22 - jnp.dot(l21, l21.T, precision=lax.Precision.HIGHEST)
    l22 = jnp.linalg.cholesky(schur)
    factor = jnp.concatenate(
        [
            jnp.concatenate([l11, jnp.zeros((kept, snaps - kept), jnp.float32)], axis=1),
            jnp.concatenate([l21, l22], axis=1),
        ],
        axis=0,
    )
    return (factor, modes)


def solution(mesh):
    in_specs = (
        P(None, ("gx", "gy")),
        P(("gx", "gy"), None),
        P(("gx", "gy")),
        P(("gx", "gy"), None),
        P(("gx", "gy"), None),
        P(),
    )
    out_specs = (P(), P(None, ("gx", "gy")))
    return jax.shard_map(body, mesh=mesh, in_specs=in_specs, out_specs=out_specs, check_vma=False)
```

```python
import functools

import jax
import jax.numpy as jnp
from jax import lax
from jax.experimental import pallas as pl
from jax.experimental.pallas import tpu as pltpu
from jax.sharding import PartitionSpec as P

RANK = 128
BLK = 128
PER = 8


def from_partner(value, axis, bit):
    mask = 2**bit
    pairs = [(source, source ^ mask) for source in range(lax.axis_size(axis))]
    return lax.ppermute(value, axis, pairs)


def all_sum(value):
    for axis in ("gx", "gy"):
        for bit in range(lax.axis_size(axis).bit_length() - 1):
            value = value + from_partner(value, axis, bit)
    return value


def lift_kernel(feeds, brick_cells, paired, blocks_ref, levels_ref, recv_ref, maps_ref, *refs):
    if paired:
        other_ref, out_ref, gram_ref = refs
    else:
        out_ref, gram_ref = refs
    step = pl.program_id(0)

    @pl.when(step == 0)
    def _():
        gram_ref[...] = jnp.zeros(gram_ref.shape, gram_ref.dtype)

    rows = out_ref.shape[0]
    for i in range(PER):
        brick = step * PER + i
        acc = None
        for n in range(feeds):
            slot = blocks_ref[brick * feeds + n]
            level = levels_ref[brick * feeds + n]
            part = jnp.dot(recv_ref[slot], maps_ref[level], preferred_element_type=jnp.float32)
            acc = part if acc is None else acc + part
        cols = slice(i * brick_cells, (i + 1) * brick_cells)
        lifted = acc.astype(out_ref.dtype)
        out_ref[:, cols] = lifted
        contract = (((1,), (1,)), ((), ()))
        if paired:
            gram_ref[:, :rows] += lax.dot_general(
                lifted, other_ref[:, cols], contract, preferred_element_type=jnp.float32
            )
            gram_ref[:, rows:] += lax.dot_general(
                lifted, lifted, contract, preferred_element_type=jnp.float32
            )
        else:
            gram_ref[...] += lax.dot_general(
                lifted, lifted, contract, preferred_element_type=jnp.float32
            )


def lift(received, blocks, levels, maps, other=None):
    slots, rows, blk = received.shape
    bricks, feeds = blocks.shape
    brick_cells = maps.shape[2]
    paired = other is not None
    in_specs = [
        pl.BlockSpec((slots, rows, blk), lambda s, b, l: (0, 0, 0)),
        pl.BlockSpec(maps.shape, lambda s, b, l: (0, 0, 0)),
    ]
    operands = [received, maps]
    gram_cols = rows
    if paired:
        in_specs.append(pl.BlockSpec((other.shape[0], PER * brick_cells), lambda s, b, l: (0, s)))
        operands.append(other)
        gram_cols = other.shape[0] + rows
    grid_spec = pltpu.PrefetchScalarGridSpec(
        num_scalar_prefetch=2,
        grid=(bricks // PER,),
        in_specs=in_specs,
        out_specs=[
            pl.BlockSpec((rows, PER * brick_cells), lambda s, b, l: (0, s)),
            pl.BlockSpec((rows, gram_cols), lambda s, b, l: (0, 0)),
        ],
    )
    cells = bricks * brick_cells
    flops = 2 * rows * blk * cells * feeds + 2 * rows * gram_cols * cells
    return pl.pallas_call(
        functools.partial(lift_kernel, feeds, brick_cells, paired),
        grid_spec=grid_spec,
        out_shape=[
            jax.ShapeDtypeStruct((rows, cells), jnp.bfloat16),
            jax.ShapeDtypeStruct((rows, gram_cols), jnp.float32),
        ],
        cost_estimate=pl.CostEstimate(
            flops=flops,
            bytes_accessed=received.size * 2 + maps.size * 2 + rows * cells * 2 * (2 if paired else 1),
            transcendentals=0,
        ),
    )(blocks.reshape(-1), levels.reshape(-1), *operands)


def gather_kernel(rows, index_ref, live_ref, cells_ref, head_ref, tail_ref, sems):
    count = head_ref.shape[0]
    blk = head_ref.shape[2]
    copies = []
    for k in range(count):
        start = pl.multiple_of(index_ref[k] * blk, blk)
        for part, dst in enumerate((head_ref, tail_ref)):
            copy = pltpu.make_async_copy(
                cells_ref.at[pl.ds(part * rows, rows), pl.ds(start, blk)],
                dst.at[k],
                sems.at[part, k],
            )
            copy.start()
            copies.append(copy)
    for copy in copies:
        copy.wait()
    for k in range(count):
        keep = live_ref[k] > 0
        for dst in (head_ref, tail_ref):
            dst[k] = jnp.where(keep, dst[k], jnp.zeros_like(dst[k]))


def gather(cells, index, live, rows):
    count = index.shape[0]
    out = jax.ShapeDtypeStruct((count, rows, BLK), cells.dtype)
    return pl.pallas_call(
        functools.partial(gather_kernel, rows),
        out_shape=[out, out],
        in_specs=[
            pl.BlockSpec(memory_space=pltpu.SMEM),
            pl.BlockSpec(memory_space=pltpu.SMEM),
            pl.BlockSpec(memory_space=pl.ANY),
        ],
        out_specs=[
            pl.BlockSpec(memory_space=pltpu.VMEM),
            pl.BlockSpec(memory_space=pltpu.VMEM),
        ],
        scratch_shapes=[pltpu.SemaphoreType.DMA((2, count))],
        cost_estimate=pl.CostEstimate(
            flops=0, bytes_accessed=4 * count * rows * BLK * 2, transcendentals=0
        ),
    )(index, live, cells)


def body(cells, send_index, send_count, prolong_block, prolong_level, prolong_maps):
    snaps = cells.shape[0]
    kept = RANK
    peers, slots = send_index.shape
    live = (jnp.arange(slots, dtype=jnp.int32)[None, :] < send_count[:, None]).reshape(-1)
    head_out, tail_out = gather(cells, send_index.reshape(-1), live.astype(jnp.int32), kept)
    head_in = lax.all_to_all(head_out, "gy", split_axis=0, concat_axis=0, tiled=True)
    head_in, tail_out = lax.optimization_barrier((head_in, tail_out))
    tail_in = lax.all_to_all(tail_out, "gy", split_axis=0, concat_axis=0, tiled=True)
    total_cells = lax.axis_size("gx") * lax.axis_size("gy") * prolong_block.shape[0] * prolong_maps.shape[2]
    head, g11 = lift(head_in, prolong_block, prolong_level, prolong_maps)
    c11 = all_sum(g11) / total_cells
    l11 = jnp.linalg.cholesky(c11)
    tail_in, l11, head = lax.optimization_barrier((tail_in, l11, head))
    tail, g2 = lift(tail_in, prolong_block, prolong_level, prolong_maps, other=head)
    g2, l11, head = lax.optimization_barrier((g2, l11, head))
    inv11 = lax.linalg.triangular_solve(
        l11, jnp.eye(kept, dtype=jnp.float32), left_side=True, lower=True
    )
    inv_top = lax.reduce_precision(inv11, exponent_bits=8, mantissa_bits=7)
    inv_hi = inv_top.astype(jnp.bfloat16)
    inv_lo = (inv11 - inv_top).astype(jnp.bfloat16)
    modes = jnp.dot(inv_hi, head, preferred_element_type=jnp.float32) + jnp.dot(
        inv_lo, head, preferred_element_type=jnp.float32
    )
    lower = all_sum(g2) / total_cells
    c21, c22 = lower[:, :kept], lower[:, kept:]
    l21 = jnp.dot(c21, inv11.T, precision=lax.Precision.HIGHEST)
    schur = c22 - jnp.dot(l21, l21.T, precision=lax.Precision.HIGHEST)
    l22 = jnp.linalg.cholesky(schur)
    factor = jnp.concatenate(
        [
            jnp.concatenate([l11, jnp.zeros((kept, snaps - kept), jnp.float32)], axis=1),
            jnp.concatenate([l21, l22], axis=1),
        ],
        axis=0,
    )
    return (factor, modes)


def solution(mesh):
    in_specs = (
        P(None, ("gx", "gy")),
        P(("gx", "gy"), None),
        P(("gx", "gy")),
        P(("gx", "gy"), None),
        P(("gx", "gy"), None),
        P(),
    )
    out_specs = (P(), P(None, ("gx", "gy")))
    return jax.shard_map(body, mesh=mesh, in_specs=in_specs, out_specs=out_specs, check_vma=False)
```

```python
import functools

import jax
import jax.numpy as jnp
from jax import lax
from jax.experimental import pallas as pl
from jax.experimental.pallas import tpu as pltpu
from jax.sharding import PartitionSpec as P

RANK = 128
BLK = 128
PER = 8


def from_partner(value, axis, bit):
    mask = 2**bit
    pairs = [(source, source ^ mask) for source in range(lax.axis_size(axis))]
    return lax.ppermute(value, axis, pairs)


def all_sum(value):
    for axis in ("gx", "gy"):
        for bit in range(lax.axis_size(axis).bit_length() - 1):
            value = value + from_partner(value, axis, bit)
    return value


def lift_kernel(feeds, brick_cells, paired, blocks_ref, levels_ref, recv_ref, maps_ref, *refs):
    if paired:
        other_ref, out_ref, gram_ref, lhs_ref, rhs_ref = refs
    else:
        out_ref, gram_ref, lhs_ref, rhs_ref = refs
    step = pl.program_id(0)

    @pl.when(step == 0)
    def _():
        gram_ref[...] = jnp.zeros(gram_ref.shape, gram_ref.dtype)

    rows = out_ref.shape[0]
    for i in range(PER):
        brick = step * PER + i
        blk = recv_ref.shape[2]
        for n in range(feeds):
            slot = blocks_ref[brick * feeds + n]
            level = levels_ref[brick * feeds + n]
            lhs_ref[:, n * blk : (n + 1) * blk] = recv_ref[slot]
            rhs_ref[n * blk : (n + 1) * blk, :] = maps_ref[level]
        acc = jnp.dot(lhs_ref[...], rhs_ref[...], preferred_element_type=jnp.float32)
        cols = slice(i * brick_cells, (i + 1) * brick_cells)
        lifted = acc.astype(out_ref.dtype)
        out_ref[:, cols] = lifted
        contract = (((1,), (1,)), ((), ()))
        if paired:
            gram_ref[:, :rows] += lax.dot_general(
                lifted, other_ref[:, cols], contract, preferred_element_type=jnp.float32
            )
            gram_ref[:, rows:] += lax.dot_general(
                lifted, lifted, contract, preferred_element_type=jnp.float32
            )
        else:
            gram_ref[...] += lax.dot_general(
                lifted, lifted, contract, preferred_element_type=jnp.float32
            )


def lift(received, blocks, levels, maps, other=None):
    slots, rows, blk = received.shape
    bricks, feeds = blocks.shape
    brick_cells = maps.shape[2]
    paired = other is not None
    in_specs = [
        pl.BlockSpec((slots, rows, blk), lambda s, b, l: (0, 0, 0)),
        pl.BlockSpec(maps.shape, lambda s, b, l: (0, 0, 0)),
    ]
    operands = [received, maps]
    gram_cols = rows
    if paired:
        in_specs.append(pl.BlockSpec((other.shape[0], PER * brick_cells), lambda s, b, l: (0, s)))
        operands.append(other)
        gram_cols = other.shape[0] + rows
    grid_spec = pltpu.PrefetchScalarGridSpec(
        num_scalar_prefetch=2,
        grid=(bricks // PER,),
        in_specs=in_specs,
        out_specs=[
            pl.BlockSpec((rows, PER * brick_cells), lambda s, b, l: (0, s)),
            pl.BlockSpec((rows, gram_cols), lambda s, b, l: (0, 0)),
        ],
        scratch_shapes=[
            pltpu.VMEM((rows, feeds * blk), received.dtype),
            pltpu.VMEM((feeds * blk, brick_cells), maps.dtype),
        ],
    )
    cells = bricks * brick_cells
    flops = 2 * rows * blk * cells * feeds + 2 * rows * gram_cols * cells
    return pl.pallas_call(
        functools.partial(lift_kernel, feeds, brick_cells, paired),
        grid_spec=grid_spec,
        out_shape=[
            jax.ShapeDtypeStruct((rows, cells), jnp.bfloat16),
            jax.ShapeDtypeStruct((rows, gram_cols), jnp.float32),
        ],
        cost_estimate=pl.CostEstimate(
            flops=flops,
            bytes_accessed=received.size * 2 + maps.size * 2 + rows * cells * 2 * (2 if paired else 1),
            transcendentals=0,
        ),
    )(blocks.reshape(-1), levels.reshape(-1), *operands)


def gather_kernel(rows, index_ref, live_ref, cells_ref, head_ref, tail_ref, sems):
    count = head_ref.shape[0]
    blk = head_ref.shape[2]
    copies = []
    for k in range(count):
        start = pl.multiple_of(index_ref[k] * blk, blk)
        for part, dst in enumerate((head_ref, tail_ref)):
            copy = pltpu.make_async_copy(
                cells_ref.at[pl.ds(part * rows, rows), pl.ds(start, blk)],
                dst.at[k],
                sems.at[part, k],
            )
            copy.start()
            copies.append(copy)
    for copy in copies:
        copy.wait()
    for k in range(count):
        keep = live_ref[k] > 0
        for dst in (head_ref, tail_ref):
            dst[k] = jnp.where(keep, dst[k], jnp.zeros_like(dst[k]))


def gather(cells, index, live, rows):
    count = index.shape[0]
    out = jax.ShapeDtypeStruct((count, rows, BLK), cells.dtype)
    return pl.pallas_call(
        functools.partial(gather_kernel, rows),
        out_shape=[out, out],
        in_specs=[
            pl.BlockSpec(memory_space=pltpu.SMEM),
            pl.BlockSpec(memory_space=pltpu.SMEM),
            pl.BlockSpec(memory_space=pl.ANY),
        ],
        out_specs=[
            pl.BlockSpec(memory_space=pltpu.VMEM),
            pl.BlockSpec(memory_space=pltpu.VMEM),
        ],
        scratch_shapes=[pltpu.SemaphoreType.DMA((2, count))],
        cost_estimate=pl.CostEstimate(
            flops=0, bytes_accessed=4 * count * rows * BLK * 2, transcendentals=0
        ),
    )(index, live, cells)


def body(cells, send_index, send_count, prolong_block, prolong_level, prolong_maps):
    snaps = cells.shape[0]
    kept = RANK
    peers, slots = send_index.shape
    live = (jnp.arange(slots, dtype=jnp.int32)[None, :] < send_count[:, None]).reshape(-1)
    head_out, tail_out = gather(cells, send_index.reshape(-1), live.astype(jnp.int32), kept)
    head_in = lax.all_to_all(head_out, "gy", split_axis=0, concat_axis=0, tiled=True)
    head_in, tail_out = lax.optimization_barrier((head_in, tail_out))
    tail_in = lax.all_to_all(tail_out, "gy", split_axis=0, concat_axis=0, tiled=True)
    total_cells = lax.axis_size("gx") * lax.axis_size("gy") * prolong_block.shape[0] * prolong_maps.shape[2]
    head, g11 = lift(head_in, prolong_block, prolong_level, prolong_maps)
    c11 = all_sum(g11) / total_cells
    l11 = jnp.linalg.cholesky(c11)
    tail_in, l11, head = lax.optimization_barrier((tail_in, l11, head))
    tail, g2 = lift(tail_in, prolong_block, prolong_level, prolong_maps, other=head)
    g2, l11, head = lax.optimization_barrier((g2, l11, head))
    inv11 = lax.linalg.triangular_solve(
        l11, jnp.eye(kept, dtype=jnp.float32), left_side=True, lower=True
    )
    inv_top = lax.reduce_precision(inv11, exponent_bits=8, mantissa_bits=7)
    inv_hi = inv_top.astype(jnp.bfloat16)
    inv_lo = (inv11 - inv_top).astype(jnp.bfloat16)
    modes = jnp.dot(inv_hi, head, preferred_element_type=jnp.float32) + jnp.dot(
        inv_lo, head, preferred_element_type=jnp.float32
    )
    lower = all_sum(g2) / total_cells
    c21, c22 = lower[:, :kept], lower[:, kept:]
    l21 = jnp.dot(c21, inv11.T, precision=lax.Precision.HIGHEST)
    schur = c22 - jnp.dot(l21, l21.T, precision=lax.Precision.HIGHEST)
    l22 = jnp.linalg.cholesky(schur)
    factor = jnp.concatenate(
        [
            jnp.concatenate([l11, jnp.zeros((kept, snaps - kept), jnp.float32)], axis=1),
            jnp.concatenate([l21, l22], axis=1),
        ],
        axis=0,
    )
    return (factor, modes)


def solution(mesh):
    in_specs = (
        P(None, ("gx", "gy")),
        P(("gx", "gy"), None),
        P(("gx", "gy")),
        P(("gx", "gy"), None),
        P(("gx", "gy"), None),
        P(),
    )
    out_specs = (P(), P(None, ("gx", "gy")))
    return jax.shard_map(body, mesh=mesh, in_specs=in_specs, out_specs=out_specs, check_vma=False)
```

```python
import functools

import jax
import jax.numpy as jnp
from jax import lax
from jax.experimental import pallas as pl
from jax.experimental.pallas import tpu as pltpu
from jax.sharding import PartitionSpec as P

RANK = 128
BLK = 128
PER = 8


def from_partner(value, axis, bit):
    mask = 2**bit
    pairs = [(source, source ^ mask) for source in range(lax.axis_size(axis))]
    return lax.ppermute(value, axis, pairs)


def all_sum(value):
    for axis in ("gx", "gy"):
        for bit in range(lax.axis_size(axis).bit_length() - 1):
            value = value + from_partner(value, axis, bit)
    return value


def lift_kernel(feeds, brick_cells, paired, blocks_ref, levels_ref, recv_ref, maps_ref, *refs):
    if paired:
        other_ref, out_ref, gram_ref, lhs_ref, rhs_ref = refs
    else:
        out_ref, gram_ref, lhs_ref, rhs_ref = refs
    step = pl.program_id(0)

    @pl.when(step == 0)
    def _():
        gram_ref[...] = jnp.zeros(gram_ref.shape, gram_ref.dtype)

    rows = out_ref.shape[0]
    for i in range(PER):
        brick = step * PER + i
        blk = recv_ref.shape[2]
        for n in range(feeds):
            slot = blocks_ref[brick * feeds + n]
            level = levels_ref[brick * feeds + n]
            lhs_ref[:, n * blk : (n + 1) * blk] = recv_ref[slot]
            rhs_ref[n * blk : (n + 1) * blk, :] = maps_ref[level]
        acc = jnp.dot(lhs_ref[...], rhs_ref[...], preferred_element_type=jnp.float32)
        cols = slice(i * brick_cells, (i + 1) * brick_cells)
        lifted = acc.astype(out_ref.dtype)
        out_ref[:, cols] = lifted
        contract = (((1,), (1,)), ((), ()))
        if paired:
            gram_ref[:, :rows] += lax.dot_general(
                lifted, other_ref[:, cols], contract, preferred_element_type=jnp.float32
            )
            gram_ref[:, rows:] += lax.dot_general(
                lifted, lifted, contract, preferred_element_type=jnp.float32
            )
        else:
            gram_ref[...] += lax.dot_general(
                lifted, lifted, contract, preferred_element_type=jnp.float32
            )


def lift(received, blocks, levels, maps, other=None):
    slots, rows, blk = received.shape
    bricks, feeds = blocks.shape
    brick_cells = maps.shape[2]
    paired = other is not None
    in_specs = [
        pl.BlockSpec((slots, rows, blk), lambda s, b, l: (0, 0, 0)),
        pl.BlockSpec(maps.shape, lambda s, b, l: (0, 0, 0)),
    ]
    operands = [received, maps]
    gram_cols = rows
    if paired:
        in_specs.append(pl.BlockSpec((other.shape[0], PER * brick_cells), lambda s, b, l: (0, s)))
        operands.append(other)
        gram_cols = other.shape[0] + rows
    grid_spec = pltpu.PrefetchScalarGridSpec(
        num_scalar_prefetch=2,
        grid=(bricks // PER,),
        in_specs=in_specs,
        out_specs=[
            pl.BlockSpec((rows, PER * brick_cells), lambda s, b, l: (0, s)),
            pl.BlockSpec((rows, gram_cols), lambda s, b, l: (0, 0)),
        ],
        scratch_shapes=[
            pltpu.VMEM((rows, feeds * blk), received.dtype),
            pltpu.VMEM((feeds * blk, brick_cells), maps.dtype),
        ],
    )
    cells = bricks * brick_cells
    flops = 2 * rows * blk * cells * feeds + 2 * rows * gram_cols * cells
    return pl.pallas_call(
        functools.partial(lift_kernel, feeds, brick_cells, paired),
        grid_spec=grid_spec,
        out_shape=[
            jax.ShapeDtypeStruct((rows, cells), jnp.bfloat16),
            jax.ShapeDtypeStruct((rows, gram_cols), jnp.float32),
        ],
        cost_estimate=pl.CostEstimate(
            flops=flops,
            bytes_accessed=received.size * 2 + maps.size * 2 + rows * cells * 2 * (2 if paired else 1),
            transcendentals=0,
        ),
    )(blocks.reshape(-1), levels.reshape(-1), *operands)


def gather_kernel(rows, index_ref, live_ref, cells_ref, head_ref, tail_ref, sems):
    count = head_ref.shape[0]
    blk = head_ref.shape[2]
    copies = []
    for k in range(count):
        start = pl.multiple_of(index_ref[k] * blk, blk)
        for part, dst in enumerate((head_ref, tail_ref)):
            copy = pltpu.make_async_copy(
                cells_ref.at[pl.ds(part * rows, rows), pl.ds(start, blk)],
                dst.at[k],
                sems.at[part, k],
            )
            copy.start()
            copies.append(copy)
    for copy in copies:
        copy.wait()
    for k in range(count):
        keep = live_ref[k] > 0
        for dst in (head_ref, tail_ref):
            dst[k] = jnp.where(keep, dst[k], jnp.zeros_like(dst[k]))


def gather(cells, index, live, rows):
    count = index.shape[0]
    out = jax.ShapeDtypeStruct((count, rows, BLK), cells.dtype)
    return pl.pallas_call(
        functools.partial(gather_kernel, rows),
        out_shape=[out, out],
        in_specs=[
            pl.BlockSpec(memory_space=pltpu.SMEM),
            pl.BlockSpec(memory_space=pltpu.SMEM),
            pl.BlockSpec(memory_space=pl.ANY),
        ],
        out_specs=[
            pl.BlockSpec(memory_space=pltpu.VMEM),
            pl.BlockSpec(memory_space=pltpu.VMEM),
        ],
        scratch_shapes=[pltpu.SemaphoreType.DMA((2, count))],
        cost_estimate=pl.CostEstimate(
            flops=0, bytes_accessed=4 * count * rows * BLK * 2, transcendentals=0
        ),
    )(index, live, cells)


def body(cells, send_index, send_count, prolong_block, prolong_level, prolong_maps):
    snaps = cells.shape[0]
    kept = RANK
    peers, slots = send_index.shape
    live = (jnp.arange(slots, dtype=jnp.int32)[None, :] < send_count[:, None]).reshape(-1)
    head_out, tail_out = gather(cells, send_index.reshape(-1), live.astype(jnp.int32), kept)
    head_in = lax.all_to_all(head_out, "gy", split_axis=0, concat_axis=0, tiled=True)
    head_in, tail_out = lax.optimization_barrier((head_in, tail_out))
    tail_in = lax.all_to_all(tail_out, "gy", split_axis=0, concat_axis=0, tiled=True)
    total_cells = lax.axis_size("gx") * lax.axis_size("gy") * prolong_block.shape[0] * prolong_maps.shape[2]
    head, g11 = lift(head_in, prolong_block, prolong_level, prolong_maps)
    c11 = all_sum(g11) / total_cells
    tail_in, c11, head = lax.optimization_barrier((tail_in, c11, head))
    tail, g2 = lift(tail_in, prolong_block, prolong_level, prolong_maps, other=head)
    g2, c11, head = lax.optimization_barrier((g2, c11, head))
    l11 = jnp.linalg.cholesky(c11)
    inv11 = lax.linalg.triangular_solve(
        l11, jnp.eye(kept, dtype=jnp.float32), left_side=True, lower=True
    )
    inv_top = lax.reduce_precision(inv11, exponent_bits=8, mantissa_bits=7)
    inv_hi = inv_top.astype(jnp.bfloat16)
    inv_lo = (inv11 - inv_top).astype(jnp.bfloat16)
    modes = jnp.dot(inv_hi, head, preferred_element_type=jnp.float32) + jnp.dot(
        inv_lo, head, preferred_element_type=jnp.float32
    )
    lower = all_sum(g2) / total_cells
    c21, c22 = lower[:, :kept], lower[:, kept:]
    l21 = jnp.dot(c21, inv11.T, precision=lax.Precision.HIGHEST)
    schur = c22 - jnp.dot(l21, l21.T, precision=lax.Precision.HIGHEST)
    l22 = jnp.linalg.cholesky(schur)
    factor = jnp.concatenate(
        [
            jnp.concatenate([l11, jnp.zeros((kept, snaps - kept), jnp.float32)], axis=1),
            jnp.concatenate([l21, l22], axis=1),
        ],
        axis=0,
    )
    return (factor, modes)


def solution(mesh):
    in_specs = (
        P(None, ("gx", "gy")),
        P(("gx", "gy"), None),
        P(("gx", "gy")),
        P(("gx", "gy"), None),
        P(("gx", "gy"), None),
        P(),
    )
    out_specs = (P(), P(None, ("gx", "gy")))
    return jax.shard_map(body, mesh=mesh, in_specs=in_specs, out_specs=out_specs, check_vma=False)
```

```python
import functools

import jax
import jax.numpy as jnp
from jax import lax
from jax.experimental import pallas as pl
from jax.experimental.pallas import tpu as pltpu
from jax.sharding import PartitionSpec as P

RANK = 128
BLK = 128
PER = 8


def from_partner(value, axis, bit):
    mask = 2**bit
    pairs = [(source, source ^ mask) for source in range(lax.axis_size(axis))]
    return lax.ppermute(value, axis, pairs)


def all_sum(value):
    for axis in ("gx", "gy"):
        for bit in range(lax.axis_size(axis).bit_length() - 1):
            value = value + from_partner(value, axis, bit)
    return value


def lift_kernel(feeds, brick_cells, paired, blocks_ref, levels_ref, recv_ref, maps_ref, *refs):
    if paired:
        other_ref, out_ref, gram_ref, lhs_ref, rhs_ref = refs
    else:
        out_ref, gram_ref, lhs_ref, rhs_ref = refs
    step = pl.program_id(0)

    @pl.when(step == 0)
    def _():
        gram_ref[...] = jnp.zeros(gram_ref.shape, gram_ref.dtype)

    rows = out_ref.shape[0]
    for i in range(PER):
        brick = step * PER + i
        blk = recv_ref.shape[2]
        for n in range(feeds):
            slot = blocks_ref[brick * feeds + n]
            level = levels_ref[brick * feeds + n]
            lhs_ref[:, n * blk : (n + 1) * blk] = recv_ref[slot]
            rhs_ref[n * blk : (n + 1) * blk, :] = maps_ref[level]
        acc = jnp.dot(lhs_ref[...], rhs_ref[...], preferred_element_type=jnp.float32)
        cols = slice(i * brick_cells, (i + 1) * brick_cells)
        lifted = acc.astype(out_ref.dtype)
        out_ref[:, cols] = lifted
        contract = (((1,), (1,)), ((), ()))
        if paired:
            gram_ref[:, :rows] += lax.dot_general(
                lifted, other_ref[:, cols], contract, preferred_element_type=jnp.float32
            )
            gram_ref[:, rows:] += lax.dot_general(
                lifted, lifted, contract, preferred_element_type=jnp.float32
            )
        else:
            gram_ref[...] += lax.dot_general(
                lifted, lifted, contract, preferred_element_type=jnp.float32
            )


def lift(received, blocks, levels, maps, other=None):
    slots, rows, blk = received.shape
    bricks, feeds = blocks.shape
    brick_cells = maps.shape[2]
    paired = other is not None
    in_specs = [
        pl.BlockSpec((slots, rows, blk), lambda s, b, l: (0, 0, 0)),
        pl.BlockSpec(maps.shape, lambda s, b, l: (0, 0, 0)),
    ]
    operands = [received, maps]
    gram_cols = rows
    if paired:
        in_specs.append(pl.BlockSpec((other.shape[0], PER * brick_cells), lambda s, b, l: (0, s)))
        operands.append(other)
        gram_cols = other.shape[0] + rows
    grid_spec = pltpu.PrefetchScalarGridSpec(
        num_scalar_prefetch=2,
        grid=(bricks // PER,),
        in_specs=in_specs,
        out_specs=[
            pl.BlockSpec((rows, PER * brick_cells), lambda s, b, l: (0, s)),
            pl.BlockSpec((rows, gram_cols), lambda s, b, l: (0, 0)),
        ],
        scratch_shapes=[
            pltpu.VMEM((rows, feeds * blk), received.dtype),
            pltpu.VMEM((feeds * blk, brick_cells), maps.dtype),
        ],
    )
    cells = bricks * brick_cells
    flops = 2 * rows * blk * cells * feeds + 2 * rows * gram_cols * cells
    return pl.pallas_call(
        functools.partial(lift_kernel, feeds, brick_cells, paired),
        grid_spec=grid_spec,
        out_shape=[
            jax.ShapeDtypeStruct((rows, cells), jnp.bfloat16),
            jax.ShapeDtypeStruct((rows, gram_cols), jnp.float32),
        ],
        cost_estimate=pl.CostEstimate(
            flops=flops,
            bytes_accessed=received.size * 2 + maps.size * 2 + rows * cells * 2 * (2 if paired else 1),
            transcendentals=0,
        ),
    )(blocks.reshape(-1), levels.reshape(-1), *operands)


def gather_kernel(first, index_ref, live_ref, cells_ref, out_ref, sems):
    count, rows, blk = out_ref.shape
    copies = []
    for k in range(count):
        start = pl.multiple_of(index_ref[k] * blk, blk)
        copy = pltpu.make_async_copy(
            cells_ref.at[pl.ds(first, rows), pl.ds(start, blk)], out_ref.at[k], sems.at[k]
        )
        copy.start()
        copies.append(copy)
    for copy in copies:
        copy.wait()
    for k in range(count):
        keep = live_ref[k] > 0
        out_ref[k] = jnp.where(keep, out_ref[k], jnp.zeros_like(out_ref[k]))


def gather(cells, index, live, first, rows):
    count = index.shape[0]
    return pl.pallas_call(
        functools.partial(gather_kernel, first),
        out_shape=jax.ShapeDtypeStruct((count, rows, BLK), cells.dtype),
        in_specs=[
            pl.BlockSpec(memory_space=pltpu.SMEM),
            pl.BlockSpec(memory_space=pltpu.SMEM),
            pl.BlockSpec(memory_space=pl.ANY),
        ],
        out_specs=pl.BlockSpec(memory_space=pltpu.VMEM),
        scratch_shapes=[pltpu.SemaphoreType.DMA((count,))],
        cost_estimate=pl.CostEstimate(
            flops=0, bytes_accessed=2 * count * rows * BLK * 2, transcendentals=0
        ),
    )(index, live, cells)


def body(cells, send_index, send_count, prolong_block, prolong_level, prolong_maps):
    snaps = cells.shape[0]
    kept = RANK
    peers, slots = send_index.shape
    live = (jnp.arange(slots, dtype=jnp.int32)[None, :] < send_count[:, None]).reshape(-1)
    flat_index, flat_live = send_index.reshape(-1), live.astype(jnp.int32)
    head_out = gather(cells, flat_index, flat_live, 0, kept)
    tail_out = gather(cells, flat_index, flat_live, kept, snaps - kept)
    head_in = lax.all_to_all(head_out, "gy", split_axis=0, concat_axis=0, tiled=True)
    head_in, tail_out = lax.optimization_barrier((head_in, tail_out))
    tail_in = lax.all_to_all(tail_out, "gy", split_axis=0, concat_axis=0, tiled=True)
    total_cells = lax.axis_size("gx") * lax.axis_size("gy") * prolong_block.shape[0] * prolong_maps.shape[2]
    head, g11 = lift(head_in, prolong_block, prolong_level, prolong_maps)
    c11 = all_sum(g11) / total_cells
    tail_in, c11, head = lax.optimization_barrier((tail_in, c11, head))
    tail, g2 = lift(tail_in, prolong_block, prolong_level, prolong_maps, other=head)
    g2, c11, head = lax.optimization_barrier((g2, c11, head))
    l11 = jnp.linalg.cholesky(c11)
    inv11 = lax.linalg.triangular_solve(
        l11, jnp.eye(kept, dtype=jnp.float32), left_side=True, lower=True
    )
    inv_top = lax.reduce_precision(inv11, exponent_bits=8, mantissa_bits=7)
    inv_hi = inv_top.astype(jnp.bfloat16)
    inv_lo = (inv11 - inv_top).astype(jnp.bfloat16)
    modes = jnp.dot(inv_hi, head, preferred_element_type=jnp.float32) + jnp.dot(
        inv_lo, head, preferred_element_type=jnp.float32
    )
    lower = all_sum(g2) / total_cells
    c21, c22 = lower[:, :kept], lower[:, kept:]
    l21 = jnp.dot(c21, inv11.T, precision=lax.Precision.HIGHEST)
    schur = c22 - jnp.dot(l21, l21.T, precision=lax.Precision.HIGHEST)
    l22 = jnp.linalg.cholesky(schur)
    factor = jnp.concatenate(
        [
            jnp.concatenate([l11, jnp.zeros((kept, snaps - kept), jnp.float32)], axis=1),
            jnp.concatenate([l21, l22], axis=1),
        ],
        axis=0,
    )
    return (factor, modes)


def solution(mesh):
    in_specs = (
        P(None, ("gx", "gy")),
        P(("gx", "gy"), None),
        P(("gx", "gy")),
        P(("gx", "gy"), None),
        P(("gx", "gy"), None),
        P(),
    )
    out_specs = (P(), P(None, ("gx", "gy")))
    return jax.shard_map(body, mesh=mesh, in_specs=in_specs, out_specs=out_specs, check_vma=False)
```

```python
import functools

import jax
import jax.numpy as jnp
from jax import lax
from jax.experimental import pallas as pl
from jax.experimental.pallas import tpu as pltpu
from jax.sharding import PartitionSpec as P

RANK = 128
BLK = 128
PER = 8


def from_partner(value, axis, bit):
    mask = 2**bit
    pairs = [(source, source ^ mask) for source in range(lax.axis_size(axis))]
    return lax.ppermute(value, axis, pairs)


def all_sum(value, axes=("gx", "gy")):
    for axis in axes:
        for bit in range(lax.axis_size(axis).bit_length() - 1):
            value = value + from_partner(value, axis, bit)
    return value


def lift_kernel(feeds, brick_cells, paired, blocks_ref, levels_ref, recv_ref, maps_ref, *refs):
    if paired:
        other_ref, out_ref, gram_ref, lhs_ref, rhs_ref = refs
    else:
        out_ref, gram_ref, lhs_ref, rhs_ref = refs
    step = pl.program_id(0)

    @pl.when(step == 0)
    def _():
        gram_ref[...] = jnp.zeros(gram_ref.shape, gram_ref.dtype)

    rows = out_ref.shape[0]
    for i in range(PER):
        brick = step * PER + i
        blk = recv_ref.shape[2]
        for n in range(feeds):
            slot = blocks_ref[brick * feeds + n]
            level = levels_ref[brick * feeds + n]
            lhs_ref[:, n * blk : (n + 1) * blk] = recv_ref[slot]
            rhs_ref[n * blk : (n + 1) * blk, :] = maps_ref[level]
        acc = jnp.dot(lhs_ref[...], rhs_ref[...], preferred_element_type=jnp.float32)
        cols = slice(i * brick_cells, (i + 1) * brick_cells)
        lifted = acc.astype(out_ref.dtype)
        out_ref[:, cols] = lifted
        contract = (((1,), (1,)), ((), ()))
        if paired:
            gram_ref[:, :rows] += lax.dot_general(
                lifted, other_ref[:, cols], contract, preferred_element_type=jnp.float32
            )
            gram_ref[:, rows:] += lax.dot_general(
                lifted, lifted, contract, preferred_element_type=jnp.float32
            )
        else:
            gram_ref[...] += lax.dot_general(
                lifted, lifted, contract, preferred_element_type=jnp.float32
            )


def lift(received, blocks, levels, maps, other=None):
    slots, rows, blk = received.shape
    bricks, feeds = blocks.shape
    brick_cells = maps.shape[2]
    paired = other is not None
    in_specs = [
        pl.BlockSpec((slots, rows, blk), lambda s, b, l: (0, 0, 0)),
        pl.BlockSpec(maps.shape, lambda s, b, l: (0, 0, 0)),
    ]
    operands = [received, maps]
    gram_cols = rows
    if paired:
        in_specs.append(pl.BlockSpec((other.shape[0], PER * brick_cells), lambda s, b, l: (0, s)))
        operands.append(other)
        gram_cols = other.shape[0] + rows
    grid_spec = pltpu.PrefetchScalarGridSpec(
        num_scalar_prefetch=2,
        grid=(bricks // PER,),
        in_specs=in_specs,
        out_specs=[
            pl.BlockSpec((rows, PER * brick_cells), lambda s, b, l: (0, s)),
            pl.BlockSpec((rows, gram_cols), lambda s, b, l: (0, 0)),
        ],
        scratch_shapes=[
            pltpu.VMEM((rows, feeds * blk), received.dtype),
            pltpu.VMEM((feeds * blk, brick_cells), maps.dtype),
        ],
    )
    cells = bricks * brick_cells
    flops = 2 * rows * blk * cells * feeds + 2 * rows * gram_cols * cells
    return pl.pallas_call(
        functools.partial(lift_kernel, feeds, brick_cells, paired),
        grid_spec=grid_spec,
        out_shape=[
            jax.ShapeDtypeStruct((rows, cells), jnp.bfloat16),
            jax.ShapeDtypeStruct((rows, gram_cols), jnp.float32),
        ],
        cost_estimate=pl.CostEstimate(
            flops=flops,
            bytes_accessed=received.size * 2 + maps.size * 2 + rows * cells * 2 * (2 if paired else 1),
            transcendentals=0,
        ),
    )(blocks.reshape(-1), levels.reshape(-1), *operands)


def gather_kernel(rows, index_ref, live_ref, cells_ref, head_ref, tail_ref, sems):
    count = head_ref.shape[0]
    blk = head_ref.shape[2]
    copies = []
    for k in range(count):
        start = pl.multiple_of(index_ref[k] * blk, blk)
        for part, dst in enumerate((head_ref, tail_ref)):
            copy = pltpu.make_async_copy(
                cells_ref.at[pl.ds(part * rows, rows), pl.ds(start, blk)],
                dst.at[k],
                sems.at[part, k],
            )
            copy.start()
            copies.append(copy)
    for copy in copies:
        copy.wait()
    for k in range(count):
        keep = live_ref[k] > 0
        for dst in (head_ref, tail_ref):
            dst[k] = jnp.where(keep, dst[k], jnp.zeros_like(dst[k]))


def gather(cells, index, live, rows):
    count = index.shape[0]
    out = jax.ShapeDtypeStruct((count, rows, BLK), cells.dtype)
    return pl.pallas_call(
        functools.partial(gather_kernel, rows),
        out_shape=[out, out],
        in_specs=[
            pl.BlockSpec(memory_space=pltpu.SMEM),
            pl.BlockSpec(memory_space=pltpu.SMEM),
            pl.BlockSpec(memory_space=pl.ANY),
        ],
        out_specs=[
            pl.BlockSpec(memory_space=pltpu.VMEM),
            pl.BlockSpec(memory_space=pltpu.VMEM),
        ],
        scratch_shapes=[pltpu.SemaphoreType.DMA((2, count))],
        cost_estimate=pl.CostEstimate(
            flops=0, bytes_accessed=4 * count * rows * BLK * 2, transcendentals=0
        ),
    )(index, live, cells)


def body(cells, send_index, send_count, prolong_block, prolong_level, prolong_maps):
    snaps = cells.shape[0]
    kept = RANK
    peers, slots = send_index.shape
    live = (jnp.arange(slots, dtype=jnp.int32)[None, :] < send_count[:, None]).reshape(-1)
    head_out, tail_out = gather(cells, send_index.reshape(-1), live.astype(jnp.int32), kept)
    head_in = lax.all_to_all(head_out, "gy", split_axis=0, concat_axis=0, tiled=True)
    head_in, tail_out = lax.optimization_barrier((head_in, tail_out))
    tail_in = lax.all_to_all(tail_out, "gy", split_axis=0, concat_axis=0, tiled=True)
    total_cells = lax.axis_size("gx") * lax.axis_size("gy") * prolong_block.shape[0] * prolong_maps.shape[2]
    head, g11 = lift(head_in, prolong_block, prolong_level, prolong_maps)
    c11 = all_sum(g11) / total_cells
    tail_in, c11, head = lax.optimization_barrier((tail_in, c11, head))
    tail, g2 = lift(tail_in, prolong_block, prolong_level, prolong_maps, other=head)
    g2, c11, head = lax.optimization_barrier((g2, c11, head))
    l11 = jnp.linalg.cholesky(c11)
    inv11 = lax.linalg.triangular_solve(
        l11, jnp.eye(kept, dtype=jnp.float32), left_side=True, lower=True
    )
    inv_top = lax.reduce_precision(inv11, exponent_bits=8, mantissa_bits=7)
    inv_hi = inv_top.astype(jnp.bfloat16)
    inv_lo = (inv11 - inv_top).astype(jnp.bfloat16)
    modes = jnp.dot(inv_hi, head, preferred_element_type=jnp.float32) + jnp.dot(
        inv_lo, head, preferred_element_type=jnp.float32
    )
    lower = all_sum(g2, ("gy", "gx")) / total_cells
    c21, c22 = lower[:, :kept], lower[:, kept:]
    l21 = jnp.dot(c21, inv11.T, precision=lax.Precision.HIGHEST)
    schur = c22 - jnp.dot(l21, l21.T, precision=lax.Precision.HIGHEST)
    l22 = jnp.linalg.cholesky(schur)
    factor = jnp.concatenate(
        [
            jnp.concatenate([l11, jnp.zeros((kept, snaps - kept), jnp.float32)], axis=1),
            jnp.concatenate([l21, l22], axis=1),
        ],
        axis=0,
    )
    return (factor, modes)


def solution(mesh):
    in_specs = (
        P(None, ("gx", "gy")),
        P(("gx", "gy"), None),
        P(("gx", "gy")),
        P(("gx", "gy"), None),
        P(("gx", "gy"), None),
        P(),
    )
    out_specs = (P(), P(None, ("gx", "gy")))
    return jax.shard_map(body, mesh=mesh, in_specs=in_specs, out_specs=out_specs, check_vma=False)
```

```python
import functools

import jax
import jax.numpy as jnp
from jax import lax
from jax.experimental import pallas as pl
from jax.experimental.pallas import tpu as pltpu
from jax.sharding import PartitionSpec as P

RANK = 128
BLK = 128
PER = 16


def from_partner(value, axis, bit):
    mask = 2**bit
    pairs = [(source, source ^ mask) for source in range(lax.axis_size(axis))]
    return lax.ppermute(value, axis, pairs)


def all_sum(value):
    for axis in ("gx", "gy"):
        for bit in range(lax.axis_size(axis).bit_length() - 1):
            value = value + from_partner(value, axis, bit)
    return value


def lift_kernel(feeds, brick_cells, paired, blocks_ref, levels_ref, recv_ref, maps_ref, *refs):
    if paired:
        other_ref, out_ref, gram_ref, lhs_ref, rhs_ref = refs
    else:
        out_ref, gram_ref, lhs_ref, rhs_ref = refs
    step = pl.program_id(0)

    @pl.when(step == 0)
    def _():
        gram_ref[...] = jnp.zeros(gram_ref.shape, gram_ref.dtype)

    rows = out_ref.shape[0]
    for i in range(PER):
        brick = step * PER + i
        blk = recv_ref.shape[2]
        for n in range(feeds):
            slot = blocks_ref[brick * feeds + n]
            level = levels_ref[brick * feeds + n]
            lhs_ref[:, n * blk : (n + 1) * blk] = recv_ref[slot]
            rhs_ref[n * blk : (n + 1) * blk, :] = maps_ref[level]
        acc = jnp.dot(lhs_ref[...], rhs_ref[...], preferred_element_type=jnp.float32)
        cols = slice(i * brick_cells, (i + 1) * brick_cells)
        lifted = acc.astype(out_ref.dtype)
        out_ref[:, cols] = lifted
        contract = (((1,), (1,)), ((), ()))
        if paired:
            gram_ref[:, :rows] += lax.dot_general(
                lifted, other_ref[:, cols], contract, preferred_element_type=jnp.float32
            )
            gram_ref[:, rows:] += lax.dot_general(
                lifted, lifted, contract, preferred_element_type=jnp.float32
            )
        else:
            gram_ref[...] += lax.dot_general(
                lifted, lifted, contract, preferred_element_type=jnp.float32
            )


def lift(received, blocks, levels, maps, other=None):
    slots, rows, blk = received.shape
    bricks, feeds = blocks.shape
    brick_cells = maps.shape[2]
    paired = other is not None
    in_specs = [
        pl.BlockSpec((slots, rows, blk), lambda s, b, l: (0, 0, 0)),
        pl.BlockSpec(maps.shape, lambda s, b, l: (0, 0, 0)),
    ]
    operands = [received, maps]
    gram_cols = rows
    if paired:
        in_specs.append(pl.BlockSpec((other.shape[0], PER * brick_cells), lambda s, b, l: (0, s)))
        operands.append(other)
        gram_cols = other.shape[0] + rows
    grid_spec = pltpu.PrefetchScalarGridSpec(
        num_scalar_prefetch=2,
        grid=(bricks // PER,),
        in_specs=in_specs,
        out_specs=[
            pl.BlockSpec((rows, PER * brick_cells), lambda s, b, l: (0, s)),
            pl.BlockSpec((rows, gram_cols), lambda s, b, l: (0, 0)),
        ],
        scratch_shapes=[
            pltpu.VMEM((rows, feeds * blk), received.dtype),
            pltpu.VMEM((feeds * blk, brick_cells), maps.dtype),
        ],
    )
    cells = bricks * brick_cells
    flops = 2 * rows * blk * cells * feeds + 2 * rows * gram_cols * cells
    return pl.pallas_call(
        functools.partial(lift_kernel, feeds, brick_cells, paired),
        grid_spec=grid_spec,
        out_shape=[
            jax.ShapeDtypeStruct((rows, cells), jnp.bfloat16),
            jax.ShapeDtypeStruct((rows, gram_cols), jnp.float32),
        ],
        cost_estimate=pl.CostEstimate(
            flops=flops,
            bytes_accessed=received.size * 2 + maps.size * 2 + rows * cells * 2 * (2 if paired else 1),
            transcendentals=0,
        ),
    )(blocks.reshape(-1), levels.reshape(-1), *operands)


def gather_kernel(rows, index_ref, live_ref, cells_ref, head_ref, tail_ref, sems):
    count = head_ref.shape[0]
    blk = head_ref.shape[2]
    copies = []
    for k in range(count):
        start = pl.multiple_of(index_ref[k] * blk, blk)
        for part, dst in enumerate((head_ref, tail_ref)):
            copy = pltpu.make_async_copy(
                cells_ref.at[pl.ds(part * rows, rows), pl.ds(start, blk)],
                dst.at[k],
                sems.at[part, k],
            )
            copy.start()
            copies.append(copy)
    for copy in copies:
        copy.wait()
    for k in range(count):
        keep = live_ref[k] > 0
        for dst in (head_ref, tail_ref):
            dst[k] = jnp.where(keep, dst[k], jnp.zeros_like(dst[k]))


def gather(cells, index, live, rows):
    count = index.shape[0]
    out = jax.ShapeDtypeStruct((count, rows, BLK), cells.dtype)
    return pl.pallas_call(
        functools.partial(gather_kernel, rows),
        out_shape=[out, out],
        in_specs=[
            pl.BlockSpec(memory_space=pltpu.SMEM),
            pl.BlockSpec(memory_space=pltpu.SMEM),
            pl.BlockSpec(memory_space=pl.ANY),
        ],
        out_specs=[
            pl.BlockSpec(memory_space=pltpu.VMEM),
            pl.BlockSpec(memory_space=pltpu.VMEM),
        ],
        scratch_shapes=[pltpu.SemaphoreType.DMA((2, count))],
        cost_estimate=pl.CostEstimate(
            flops=0, bytes_accessed=4 * count * rows * BLK * 2, transcendentals=0
        ),
    )(index, live, cells)


def body(cells, send_index, send_count, prolong_block, prolong_level, prolong_maps):
    snaps = cells.shape[0]
    kept = RANK
    peers, slots = send_index.shape
    live = (jnp.arange(slots, dtype=jnp.int32)[None, :] < send_count[:, None]).reshape(-1)
    head_out, tail_out = gather(cells, send_index.reshape(-1), live.astype(jnp.int32), kept)
    head_in = lax.all_to_all(head_out, "gy", split_axis=0, concat_axis=0, tiled=True)
    head_in, tail_out = lax.optimization_barrier((head_in, tail_out))
    tail_in = lax.all_to_all(tail_out, "gy", split_axis=0, concat_axis=0, tiled=True)
    total_cells = lax.axis_size("gx") * lax.axis_size("gy") * prolong_block.shape[0] * prolong_maps.shape[2]
    head, g11 = lift(head_in, prolong_block, prolong_level, prolong_maps)
    c11 = all_sum(g11) / total_cells
    tail_in, c11, head = lax.optimization_barrier((tail_in, c11, head))
    tail, g2 = lift(tail_in, prolong_block, prolong_level, prolong_maps, other=head)
    g2, c11, head = lax.optimization_barrier((g2, c11, head))
    l11 = jnp.linalg.cholesky(c11)
    inv11 = lax.linalg.triangular_solve(
        l11, jnp.eye(kept, dtype=jnp.float32), left_side=True, lower=True
    )
    inv_top = lax.reduce_precision(inv11, exponent_bits=8, mantissa_bits=7)
    inv_hi = inv_top.astype(jnp.bfloat16)
    inv_lo = (inv11 - inv_top).astype(jnp.bfloat16)
    modes = jnp.dot(inv_hi, head, preferred_element_type=jnp.float32) + jnp.dot(
        inv_lo, head, preferred_element_type=jnp.float32
    )
    lower = all_sum(g2) / total_cells
    c21, c22 = lower[:, :kept], lower[:, kept:]
    l21 = jnp.dot(c21, inv11.T, precision=lax.Precision.HIGHEST)
    schur = c22 - jnp.dot(l21, l21.T, precision=lax.Precision.HIGHEST)
    l22 = jnp.linalg.cholesky(schur)
    factor = jnp.concatenate(
        [
            jnp.concatenate([l11, jnp.zeros((kept, snaps - kept), jnp.float32)], axis=1),
            jnp.concatenate([l21, l22], axis=1),
        ],
        axis=0,
    )
    return (factor, modes)


def solution(mesh):
    in_specs = (
        P(None, ("gx", "gy")),
        P(("gx", "gy"), None),
        P(("gx", "gy")),
        P(("gx", "gy"), None),
        P(("gx", "gy"), None),
        P(),
    )
    out_specs = (P(), P(None, ("gx", "gy")))
    return jax.shard_map(body, mesh=mesh, in_specs=in_specs, out_specs=out_specs, check_vma=False)
```
